128 devices in a mesh: af: 128 (over z, x, y, core).
Axes of the slice: x: 4, y: 4, z: 4, core: 2. Of those that a mesh axis runs over, the one named last changes fastest.
Arguments:
- reflection: bfloat16 [2, 256, 1536, 1536], P(None, 'af'), may hold values from -0.15625 to 0.15625
- focus_plus: float32 [32, 1536, 512], P(None, 'af'), may hold values from -6 to 6
- focus_direct: float32 [32, 1536, 512], P(None, 'af'), may hold values from -6 to 6
- onset_index: int32 [32, 1536], P(None, 'af'), may hold values from 64 to 256
Outputs:
- focus_minus: float32 [32, 1536, 512], P(None, 'af')
- focus_next: float32 [32, 1536, 512], P(None, 'af')
The draws below stay inside these ranges and needn't reach their ends.
Inputs may be any that keep to these rules, and one draw needn't show every extreme that they name: onset_index[p, r] is the half-width in samples, around sample 512/2, of the window of focal point p at station r.
All inputs are finite; a program needn't handle non-finite values.
Results may differ from the reference program's by a relative error of at most 0.0029.
Values may be sent and summed in bfloat16 or wider, within the bound.
No kernel may reach another device: no remote copies, remote signals or barrier semaphores. Data moves between devices by JAX's collectives and lax.ppermute only.
A program may use at most 128 MiB of HBM per device.

```python
import math
import jax
import jax.numpy as jnp
from jax import lax

STATIONS = 1536
NFREQ = 256
NT = 512
POINTS = 32


def touch_ends(array, stream_key, low, largest):
    dims = array.shape
    index_at = [jax.random.randint(jax.random.fold_in(stream_key, axis), (), 0, dims[axis]) for axis in range(len(dims))]
    array = array.at[tuple(index_at)].set(low)
    longest = dims.index(max(dims))
    index_at[longest] = (index_at[longest] + 1) % dims[longest]
    return array.at[tuple(index_at)].set(largest)


def block_scale(stream_key, dims, split, least, high):
    loudness, own = 1.0, jax.random.fold_in(stream_key, 6)
    for position, shards_of in split:
        steps = jnp.exp(jax.random.uniform(jax.random.fold_in(own, position), (shards_of,), jnp.float32, least / len(split), high / len(split)))
        loudness = loudness * jnp.repeat(steps, dims[position] // shards_of).reshape([-1 if axis == position else 1 for axis in range(len(dims))])
    return loudness


def normal_values(own_key, extent, scale, most, shards=(), held_as=jnp.bfloat16):
    drawn = scale * jax.random.normal(own_key, extent, jnp.float32)
    if shards:
        drawn = drawn * block_scale(own_key, extent, shards, -0.22, 0.18)
    return jnp.clip(drawn, -most, most).astype(held_as)


def setup_inputs(seed: int = 0) -> dict:
    arg_keys = jax.random.split(jax.random.key(seed), 5)
    return {
        "reflection": normal_values(arg_keys[0], (2, NFREQ, STATIONS, STATIONS), STATIONS ** -0.5, 0.15625, ((1, 128),)),
        "focus_plus": normal_values(arg_keys[1], (POINTS, STATIONS, NT), 1.0, 6.0, ((1, 128),), jnp.float32),
        "focus_direct": normal_values(arg_keys[2], (POINTS, STATIONS, NT), 1.0, 6.0, ((1, 128),), jnp.float32),
        "onset_index": touch_ends(jax.random.randint(arg_keys[3], (POINTS, STATIONS), NT // 8, NT // 2 + 1), jax.random.fold_in(arg_keys[3], 1), NT // 8, (NT // 2 + 1) - 1).astype(jnp.int32),
    }


def base_table():
    freq_index = jnp.arange(NFREQ, dtype=jnp.int32)
    time_index = jnp.arange(NT, dtype=jnp.int32)
    phase = freq_index[:, None] * time_index[None, :] % NT
    angle = phase.astype(jnp.float32) * (2.0 * math.pi / NT)
    return (jnp.cos(angle), jnp.sin(angle))

def spectra_of(traces):
    cosine, sine_part = base_table()
    forward_scale = 1.0 / math.sqrt(NT)
    real_part = jnp.einsum('pst,kt->kps', traces, cosine, precision=lax.Precision.HIGHEST) * forward_scale
    imag_part = -jnp.einsum('pst,kt->kps', traces, sine_part, precision=lax.Precision.HIGHEST) * forward_scale
    return (real_part.astype(jnp.bfloat16), imag_part.astype(jnp.bfloat16))

def traces_of(real_part, imag_part):
    cosine, sine_part = base_table()
    inverse_scale = 1.0 / math.sqrt(NFREQ)
    total = jnp.einsum('kps,kt->pst', real_part, cosine, precision=lax.Precision.HIGHEST)
    total = total - jnp.einsum('kps,kt->pst', imag_part, sine_part, precision=lax.Precision.HIGHEST)
    return total * inverse_scale

def windowed(traces, onset_index):
    time_index = jnp.arange(NT, dtype=jnp.int32)
    distance = jnp.abs(time_index - NT // 2)
    keep = distance[None, None, :] < onset_index[:, :, None]
    return jnp.where(keep, traces, jnp.zeros_like(traces))

def forward_product(reflection, real_part, imag_part):

    def one_freq(pieces):
        reflect_real, reflect_imag, spectra_real, spectra_imag = pieces
        out_real = jnp.dot(spectra_real, reflect_real.T, preferred_element_type=jnp.float32) - jnp.dot(spectra_imag, reflect_imag.T, preferred_element_type=jnp.float32)
        out_imag = jnp.dot(spectra_imag, reflect_real.T, preferred_element_type=jnp.float32) + jnp.dot(spectra_real, reflect_imag.T, preferred_element_type=jnp.float32)
        return (out_real, out_imag)
    return lax.map(one_freq, (reflection[0], reflection[1], real_part, imag_part))

def adjoint_product(reflection, real_part, imag_part):

    def one_freq(pieces):
        reflect_real, reflect_imag, spectra_real, spectra_imag = pieces
        out_real = jnp.dot(spectra_real, reflect_real, preferred_element_type=jnp.float32) + jnp.dot(spectra_imag, reflect_imag, preferred_element_type=jnp.float32)
        out_imag = jnp.dot(spectra_imag, reflect_real, preferred_element_type=jnp.float32) - jnp.dot(spectra_real, reflect_imag, preferred_element_type=jnp.float32)
        return (out_real, out_imag)
    return lax.map(one_freq, (reflection[0], reflection[1], real_part, imag_part))

def reference(reflection, focus_plus, focus_direct, onset_index):
    plus_real, plus_imag = spectra_of(focus_plus)
    image_real, image_imag = forward_product(reflection, plus_real, plus_imag)
    focus_minus = windowed(traces_of(image_real, image_imag), onset_index)
    minus_real, minus_imag = spectra_of(focus_minus)
    back_real, back_imag = adjoint_product(reflection, minus_real, minus_imag)
    focus_next = focus_direct + windowed(traces_of(back_real, back_imag), onset_index)
    return (focus_minus, focus_next)
```

```python
import math

import numpy as np

import jax
import jax.numpy as jnp
from jax import lax
from jax.sharding import PartitionSpec as P

NFREQ = 256
NT = 512


def base_table(nfreq, ntime):
    phase = (np.arange(nfreq)[:, None] * np.arange(ntime)[None, :]) % ntime
    angle = phase.astype(np.float64) * (2.0 * math.pi / ntime)
    table = np.stack([np.cos(angle), -np.sin(angle)], 1).reshape(2 * nfreq, ntime)
    return jnp.asarray(table.astype(np.float32))


def spectra_of(traces, table, groups):
    points, stations_dev, ntime = traces.shape
    mixed = lax.dot_general(
        traces,
        table,
        (((2,), (1,)), ((), ())),
        precision=lax.Precision.HIGHEST,
        preferred_element_type=jnp.float32,
    )
    scaled = (mixed * (1.0 / math.sqrt(ntime))).astype(jnp.bfloat16)
    local = table.shape[0] // 2 // groups
    scaled = scaled.reshape(points, stations_dev, groups, local, 2)
    scaled = scaled.transpose(2, 1, 3, 4, 0)
    return scaled.reshape(groups, stations_dev, local * 2 * points)


def traces_of(arrived, table, points):
    groups, stations_dev, lanes = arrived.shape
    local = lanes // (2 * points)
    spec = arrived.reshape(groups, stations_dev, local, 2, points)
    tab = table.reshape(groups, local, 2, table.shape[1])
    mixed = lax.dot_general(
        spec,
        tab,
        (((0, 2, 3), (0, 1, 2)), ((), ())),
        precision=lax.Precision.HIGHEST,
        preferred_element_type=jnp.float32,
    )
    scaled = mixed * (1.0 / math.sqrt(table.shape[0] // 2))
    return scaled.transpose(1, 0, 2)


def windowed(traces, onset_index):
    time_index = jnp.arange(traces.shape[2], dtype=jnp.int32)
    distance = jnp.abs(time_index - traces.shape[2] // 2)
    keep = distance[None, None, :] < onset_index[:, :, None]
    return jnp.where(keep, traces, jnp.zeros_like(traces))


def split_spectra(arrived, points):
    groups, stations_dev, lanes = arrived.shape
    local = lanes // (2 * points)
    spec = arrived.reshape(groups * stations_dev, local, 2, points).transpose(1, 0, 2, 3)
    real = spec[:, :, 0]
    imag = spec[:, :, 1]
    return real, imag, local


def forward_product(reflection, arrived, points):
    real, imag, local = split_spectra(arrived, points)
    both = jnp.concatenate([real, imag], 2)
    turned = jnp.concatenate([-imag, real], 2)
    out = jnp.einsum("ksr,krq->ksq", reflection[0], both, preferred_element_type=jnp.float32)
    out = out + jnp.einsum("ksr,krq->ksq", reflection[1], turned, preferred_element_type=jnp.float32)
    return out


def adjoint_product(reflection, arrived, points):
    real, imag, local = split_spectra(arrived, points)
    both = jnp.concatenate([real, imag], 2)
    turned = jnp.concatenate([imag, -real], 2)
    out = jnp.einsum("ksr,ksq->krq", reflection[0], both, preferred_element_type=jnp.float32)
    out = out + jnp.einsum("ksr,ksq->krq", reflection[1], turned, preferred_element_type=jnp.float32)
    return out


def to_owners(product, groups):
    local, stations, lanes = product.shape
    out = product.transpose(1, 0, 2).reshape(groups, stations // groups, local * lanes)
    return out


def per_device(reflection, focus_plus, focus_direct, onset_index):
    groups = lax.axis_size("af")
    points = focus_plus.shape[0]
    table = base_table(NFREQ, NT)

    def convolve(spectra, product):
        arrived = lax.all_to_all(spectra, "af", 0, 0, tiled=True)
        result = to_owners(product(reflection, arrived, points), groups)
        return lax.all_to_all(result, "af", 0, 0, tiled=True)

    images = convolve(spectra_of(focus_plus, table, groups), forward_product)
    focus_minus = windowed(traces_of(images, table, points), onset_index)
    returns = convolve(spectra_of(focus_minus, table, groups), adjoint_product)
    focus_next = focus_direct + windowed(traces_of(returns, table, points), onset_index)
    return (focus_minus, focus_next)


def solution(mesh):
    return jax.shard_map(
        per_device,
        mesh=mesh,
        in_specs=(
            P(None, "af", None, None),
            P(None, "af", None),
            P(None, "af", None),
            P(None, "af"),
        ),
        out_specs=(P(None, "af", None), P(None, "af", None)),
        check_vma=False,
    )
```

```python
import math

import numpy as np

import jax
import jax.numpy as jnp
from jax import lax
from jax.experimental import pallas as pl
from jax.experimental.pallas import tpu as pltpu
from jax.sharding import PartitionSpec as P

NFREQ = 256
NT = 512
TS = 128


def _fwd_kernel(x_ref, r_ref, o_ref, xp_ref):
    @pl.when(pl.program_id(0) == 0)
    def _():
        x = x_ref[...].astype(jnp.float32)
        lane = lax.broadcasted_iota(jnp.int32, x.shape, 1)
        first = (lane % 64) < 32
        xp = jnp.where(first, -pltpu.roll(x, 96, 1), pltpu.roll(x, 32, 1))
        xp_ref[...] = xp.astype(jnp.bfloat16)

    x = x_ref[...]
    xp = xp_ref[...]
    a0 = jnp.dot(r_ref[0, 0], x, preferred_element_type=jnp.float32)
    a0 = a0 + jnp.dot(r_ref[1, 0], xp, preferred_element_type=jnp.float32)
    a1 = jnp.dot(r_ref[0, 1], x, preferred_element_type=jnp.float32)
    a1 = a1 + jnp.dot(r_ref[1, 1], xp, preferred_element_type=jnp.float32)
    lane = lax.broadcasted_iota(jnp.int32, a0.shape, 1)
    o_ref[...] = jnp.where(lane < 64, a0, a1)


def forward_kernel(reflection, x):
    stations = x.shape[0]
    return pl.pallas_call(
        _fwd_kernel,
        grid=(stations // TS,),
        in_specs=[
            pl.BlockSpec((stations, 128), lambda i: (0, 0)),
            pl.BlockSpec((2, 2, TS, stations), lambda i: (0, 0, i, 0)),
        ],
        out_specs=pl.BlockSpec((TS, 128), lambda i: (i, 0)),
        out_shape=jax.ShapeDtypeStruct((stations, 128), jnp.float32),
        scratch_shapes=[pltpu.VMEM((stations, 128), jnp.bfloat16)],
    )(x, reflection)


def _adj_kernel(y_ref, r_ref, o_ref, yt_ref, ytp_ref, acc_ref):
    i = pl.program_id(0)

    @pl.when(i == 0)
    def _():
        yt = y_ref[...].astype(jnp.float32).T
        ytp = jnp.concatenate(
            [yt[32:64], -yt[0:32], yt[96:128], -yt[64:96]], 0)
        yt_ref[...] = yt.astype(jnp.bfloat16)
        ytp_ref[...] = ytp.astype(jnp.bfloat16)
        acc_ref[...] = jnp.zeros(acc_ref.shape, jnp.float32)

    off = pl.multiple_of(i * TS, TS)
    yt = yt_ref[:, pl.ds(off, TS)]
    ytp = ytp_ref[:, pl.ds(off, TS)]
    a0 = jnp.dot(yt[0:64], r_ref[0, 0], preferred_element_type=jnp.float32)
    a0 = a0 + jnp.dot(ytp[0:64], r_ref[1, 0], preferred_element_type=jnp.float32)
    a1 = jnp.dot(yt[64:128], r_ref[0, 1], preferred_element_type=jnp.float32)
    a1 = a1 + jnp.dot(ytp[64:128], r_ref[1, 1], preferred_element_type=jnp.float32)
    acc_ref[...] += jnp.concatenate([a0, a1], 0)

    @pl.when(i == pl.num_programs(0) - 1)
    def _():
        o_ref[...] = acc_ref[...].T


def adjoint_kernel(reflection, y):
    stations = y.shape[0]
    return pl.pallas_call(
        _adj_kernel,
        grid=(stations // TS,),
        in_specs=[
            pl.BlockSpec((stations, 128), lambda i: (0, 0)),
            pl.BlockSpec((2, 2, TS, stations), lambda i: (0, 0, i, 0)),
        ],
        out_specs=pl.BlockSpec((stations, 128), lambda i: (0, 0)),
        out_shape=jax.ShapeDtypeStruct((stations, 128), jnp.float32),
        scratch_shapes=[
            pltpu.VMEM((128, stations), jnp.bfloat16),
            pltpu.VMEM((128, stations), jnp.bfloat16),
            pltpu.VMEM((128, stations), jnp.float32),
        ],
    )(y, reflection)


def base_table(nfreq, ntime):
    phase = (np.arange(nfreq)[:, None] * np.arange(ntime)[None, :]) % ntime
    angle = phase.astype(np.float64) * (2.0 * math.pi / ntime)
    table = np.stack([np.cos(angle), -np.sin(angle)], 1).reshape(2 * nfreq, ntime)
    return jnp.asarray(table.astype(np.float32))


def spectra_of(traces, table, groups):
    points, stations_dev, ntime = traces.shape
    mixed = lax.dot_general(
        traces,
        table,
        (((2,), (1,)), ((), ())),
        precision=lax.Precision.HIGHEST,
        preferred_element_type=jnp.float32,
    )
    scaled = (mixed * (1.0 / math.sqrt(ntime))).astype(jnp.bfloat16)
    local = table.shape[0] // 2 // groups
    scaled = scaled.reshape(points, stations_dev, groups, local, 2)
    scaled = scaled.transpose(2, 1, 3, 4, 0)
    return scaled.reshape(groups, stations_dev, local * 2 * points)


def traces_of(arrived, table, points):
    groups, stations_dev, lanes = arrived.shape
    local = lanes // (2 * points)
    spec = arrived.reshape(groups, stations_dev, local, 2, points)
    tab = table.reshape(groups, local, 2, table.shape[1])
    mixed = lax.dot_general(
        spec,
        tab,
        (((0, 2, 3), (0, 1, 2)), ((), ())),
        precision=lax.Precision.HIGHEST,
        preferred_element_type=jnp.float32,
    )
    scaled = mixed * (1.0 / math.sqrt(table.shape[0] // 2))
    return scaled.transpose(1, 0, 2)


def windowed(traces, onset_index):
    time_index = jnp.arange(traces.shape[2], dtype=jnp.int32)
    distance = jnp.abs(time_index - traces.shape[2] // 2)
    keep = distance[None, None, :] < onset_index[:, :, None]
    return jnp.where(keep, traces, jnp.zeros_like(traces))


def per_device(reflection, focus_plus, focus_direct, onset_index):
    groups = lax.axis_size("af")
    points = focus_plus.shape[0]
    table = base_table(NFREQ, NT)

    def convolve(spectra, product):
        arrived = lax.all_to_all(spectra, "af", 0, 0, tiled=True)
        stations = arrived.shape[0] * arrived.shape[1]
        result = product(reflection, arrived.reshape(stations, arrived.shape[2]))
        result = result.reshape(arrived.shape)
        return lax.all_to_all(result, "af", 0, 0, tiled=True)

    images = convolve(spectra_of(focus_plus, table, groups), forward_kernel)
    focus_minus = windowed(traces_of(images, table, points), onset_index)
    returns = convolve(spectra_of(focus_minus, table, groups), adjoint_kernel)
    focus_next = focus_direct + windowed(traces_of(returns, table, points), onset_index)
    return (focus_minus, focus_next)


def solution(mesh):
    return jax.shard_map(
        per_device,
        mesh=mesh,
        in_specs=(
            P(None, "af", None, None),
            P(None, "af", None),
            P(None, "af", None),
            P(None, "af"),
        ),
        out_specs=(P(None, "af", None), P(None, "af", None)),
        check_vma=False,
    )
```

```python
import math

import numpy as np

import jax
import jax.numpy as jnp
from jax import lax
from jax.experimental import pallas as pl
from jax.experimental.pallas import tpu as pltpu
from jax.sharding import PartitionSpec as P

NFREQ = 256
NT = 512
TS = 512


def _partner(x, negate_first):
    x = x.astype(jnp.float32)
    lane = lax.broadcasted_iota(jnp.int32, x.shape, 1)
    first = (lane % 64) < 32
    ahead = pltpu.roll(x, 96, 1)
    behind = pltpu.roll(x, 32, 1)
    if negate_first:
        out = jnp.where(first, -ahead, behind)
    else:
        out = jnp.where(first, ahead, -behind)
    return out.astype(jnp.bfloat16)


def _fwd_kernel(x_ref, r_ref, o_ref, xp_ref):
    @pl.when(pl.program_id(0) == 0)
    def _():
        xp_ref[...] = _partner(x_ref[...], True)

    parts = []
    for kl in range(2):
        x = x_ref[:, kl * 64:(kl + 1) * 64]
        xp = xp_ref[:, kl * 64:(kl + 1) * 64]
        a = jnp.dot(r_ref[0, kl], x, preferred_element_type=jnp.float32)
        a = a + jnp.dot(r_ref[1, kl], xp, preferred_element_type=jnp.float32)
        parts.append(a)
    o_ref[...] = jnp.concatenate(parts, 1)


def forward_kernel(reflection, x):
    stations = x.shape[0]
    return pl.pallas_call(
        _fwd_kernel,
        grid=(stations // TS,),
        in_specs=[
            pl.BlockSpec((stations, 128), lambda i: (0, 0)),
            pl.BlockSpec((2, 2, TS, stations), lambda i: (0, 0, i, 0)),
        ],
        out_specs=pl.BlockSpec((TS, 128), lambda i: (i, 0)),
        out_shape=jax.ShapeDtypeStruct((stations, 128), jnp.float32),
        scratch_shapes=[pltpu.VMEM((stations, 128), jnp.bfloat16)],
    )(x, reflection)


def _adj_kernel(y_ref, r_ref, o_ref, yp_ref, acc_ref):
    i = pl.program_id(0)

    @pl.when(i == 0)
    def _():
        yp_ref[...] = _partner(y_ref[...], False)
        acc_ref[...] = jnp.zeros(acc_ref.shape, jnp.float32)

    off = pl.multiple_of(i * TS, TS)
    y = y_ref[pl.ds(off, TS), :]
    yp = yp_ref[pl.ds(off, TS), :]
    dims = (((0,), (0,)), ((), ()))
    parts = []
    for kl in range(2):
        a = lax.dot_general(r_ref[0, kl], y[:, kl * 64:(kl + 1) * 64], dims,
                            preferred_element_type=jnp.float32)
        a = a + lax.dot_general(r_ref[1, kl], yp[:, kl * 64:(kl + 1) * 64], dims,
                                preferred_element_type=jnp.float32)
        parts.append(a)
    acc_ref[...] += jnp.concatenate(parts, 1)

    @pl.when(i == pl.num_programs(0) - 1)
    def _():
        o_ref[...] = acc_ref[...]


def adjoint_kernel(reflection, y):
    stations = y.shape[0]
    return pl.pallas_call(
        _adj_kernel,
        grid=(stations // TS,),
        in_specs=[
            pl.BlockSpec((stations, 128), lambda i: (0, 0)),
            pl.BlockSpec((2, 2, TS, stations), lambda i: (0, 0, i, 0)),
        ],
        out_specs=pl.BlockSpec((stations, 128), lambda i: (0, 0)),
        out_shape=jax.ShapeDtypeStruct((stations, 128), jnp.float32),
        scratch_shapes=[
            pltpu.VMEM((stations, 128), jnp.bfloat16),
            pltpu.VMEM((stations, 128), jnp.float32),
        ],
    )(y, reflection)


def base_table(nfreq, ntime):
    phase = (np.arange(nfreq)[:, None] * np.arange(ntime)[None, :]) % ntime
    angle = phase.astype(np.float64) * (2.0 * math.pi / ntime)
    table = np.stack([np.cos(angle), -np.sin(angle)], 1).reshape(2 * nfreq, ntime)
    return jnp.asarray(table.astype(np.float32))


def spectra_of(traces, table, groups):
    points, stations_dev, ntime = traces.shape
    mixed = lax.dot_general(
        traces,
        table,
        (((2,), (1,)), ((), ())),
        precision=lax.Precision.HIGHEST,
        preferred_element_type=jnp.float32,
    )
    scaled = (mixed * (1.0 / math.sqrt(ntime))).astype(jnp.bfloat16)
    local = table.shape[0] // 2 // groups
    scaled = scaled.reshape(points, stations_dev, groups, local, 2)
    scaled = scaled.transpose(2, 1, 3, 4, 0)
    return scaled.reshape(groups, stations_dev, local * 2 * points)


def traces_of(arrived, table, points):
    groups, stations_dev, lanes = arrived.shape
    local = lanes // (2 * points)
    spec = arrived.reshape(groups, stations_dev, local, 2, points)
    tab = table.reshape(groups, local, 2, table.shape[1])
    mixed = lax.dot_general(
        spec,
        tab,
        (((0, 2, 3), (0, 1, 2)), ((), ())),
        precision=lax.Precision.HIGHEST,
        preferred_element_type=jnp.float32,
    )
    scaled = mixed * (1.0 / math.sqrt(table.shape[0] // 2))
    return scaled.transpose(1, 0, 2)


def windowed(traces, onset_index):
    time_index = jnp.arange(traces.shape[2], dtype=jnp.int32)
    distance = jnp.abs(time_index - traces.shape[2] // 2)
    keep = distance[None, None, :] < onset_index[:, :, None]
    return jnp.where(keep, traces, jnp.zeros_like(traces))


def per_device(reflection, focus_plus, focus_direct, onset_index):
    groups = lax.axis_size("af")
    points = focus_plus.shape[0]
    table = base_table(NFREQ, NT)

    def convolve(spectra, product):
        arrived = lax.all_to_all(spectra, "af", 0, 0, tiled=True)
        stations = arrived.shape[0] * arrived.shape[1]
        result = product(reflection, arrived.reshape(stations, arrived.shape[2]))
        result = result.reshape(arrived.shape)
        return lax.all_to_all(result, "af", 0, 0, tiled=True)

    images = convolve(spectra_of(focus_plus, table, groups), forward_kernel)
    focus_minus = windowed(traces_of(images, table, points), onset_index)
    returns = convolve(spectra_of(focus_minus, table, groups), adjoint_kernel)
    focus_next = focus_direct + windowed(traces_of(returns, table, points), onset_index)
    return (focus_minus, focus_next)


def solution(mesh):
    return jax.shard_map(
        per_device,
        mesh=mesh,
        in_specs=(
            P(None, "af", None, None),
            P(None, "af", None),
            P(None, "af", None),
            P(None, "af"),
        ),
        out_specs=(P(None, "af", None), P(None, "af", None)),
        check_vma=False,
    )
```

```python
import math

import numpy as np

import jax
import jax.numpy as jnp
from jax import lax
from jax.experimental import pallas as pl
from jax.experimental.pallas import tpu as pltpu
from jax.sharding import PartitionSpec as P

NFREQ = 256
NT = 512
TS = 512


def _partner(x, negate_first):
    x = x.astype(jnp.float32)
    lane = lax.broadcasted_iota(jnp.int32, x.shape, 1)
    first = (lane % 64) < 32
    ahead = pltpu.roll(x, 96, 1)
    behind = pltpu.roll(x, 32, 1)
    if negate_first:
        out = jnp.where(first, -ahead, behind)
    else:
        out = jnp.where(first, ahead, -behind)
    return out.astype(jnp.bfloat16)


def _fwd_kernel(x_ref, r_ref, o_ref, xp_ref):
    @pl.when(pl.program_id(0) == 0)
    def _():
        xp_ref[...] = _partner(x_ref[...], True)

    parts = []
    for kl in range(2):
        x = x_ref[:, kl * 64:(kl + 1) * 64]
        xp = xp_ref[:, kl * 64:(kl + 1) * 64]
        a = jnp.dot(r_ref[0, kl], x, preferred_element_type=jnp.float32)
        a = a + jnp.dot(r_ref[1, kl], xp, preferred_element_type=jnp.float32)
        parts.append(a)
    o_ref[...] = jnp.concatenate(parts, 1)


def forward_kernel(reflection, x):
    stations = x.shape[0]
    return pl.pallas_call(
        _fwd_kernel,
        grid=(stations // TS,),
        in_specs=[
            pl.BlockSpec((stations, 128), lambda i: (0, 0)),
            pl.BlockSpec((2, 2, TS, stations), lambda i: (0, 0, i, 0)),
        ],
        out_specs=pl.BlockSpec((TS, 128), lambda i: (i, 0)),
        out_shape=jax.ShapeDtypeStruct((stations, 128), jnp.float32),
        scratch_shapes=[pltpu.VMEM((stations, 128), jnp.bfloat16)],
    )(x, reflection)


def _adj_kernel(y_ref, r_ref, o_ref, yp_ref, acc_ref):
    i = pl.program_id(0)

    @pl.when(i == 0)
    def _():
        yp_ref[...] = _partner(y_ref[...], False)
        acc_ref[...] = jnp.zeros(acc_ref.shape, jnp.float32)

    off = pl.multiple_of(i * TS, TS)
    y = y_ref[pl.ds(off, TS), :]
    yp = yp_ref[pl.ds(off, TS), :]
    dims = (((0,), (0,)), ((), ()))
    parts = []
    for kl in range(2):
        a = lax.dot_general(r_ref[0, kl], y[:, kl * 64:(kl + 1) * 64], dims,
                            preferred_element_type=jnp.float32)
        a = a + lax.dot_general(r_ref[1, kl], yp[:, kl * 64:(kl + 1) * 64], dims,
                                preferred_element_type=jnp.float32)
        parts.append(a)
    acc_ref[...] += jnp.concatenate(parts, 1)

    @pl.when(i == pl.num_programs(0) - 1)
    def _():
        o_ref[...] = acc_ref[...]


def adjoint_kernel(reflection, y):
    stations = y.shape[0]
    return pl.pallas_call(
        _adj_kernel,
        grid=(stations // TS,),
        in_specs=[
            pl.BlockSpec((stations, 128), lambda i: (0, 0)),
            pl.BlockSpec((2, 2, TS, stations), lambda i: (0, 0, i, 0)),
        ],
        out_specs=pl.BlockSpec((stations, 128), lambda i: (0, 0)),
        out_shape=jax.ShapeDtypeStruct((stations, 128), jnp.float32),
        scratch_shapes=[
            pltpu.VMEM((stations, 128), jnp.bfloat16),
            pltpu.VMEM((stations, 128), jnp.float32),
        ],
    )(y, reflection)


def base_table(nfreq, ntime):
    phase = (np.arange(nfreq)[:, None] * np.arange(ntime)[None, :]) % ntime
    angle = phase.astype(np.float64) * (2.0 * math.pi / ntime)
    table = np.stack([np.cos(angle), -np.sin(angle)], 1).reshape(2 * nfreq, ntime)
    return jnp.asarray(table.astype(np.float32))


def spectra_of(traces, table, groups):
    points, stations_dev, ntime = traces.shape
    mixed = lax.dot_general(
        traces,
        table,
        (((2,), (1,)), ((), ())),
        precision=lax.Precision.HIGHEST,
        preferred_element_type=jnp.float32,
    )
    scaled = (mixed * (1.0 / math.sqrt(ntime))).astype(jnp.bfloat16)
    local = table.shape[0] // 2 // groups
    scaled = scaled.reshape(points, stations_dev, groups, local, 2)
    scaled = scaled.transpose(2, 1, 3, 4, 0)
    return scaled.reshape(groups, 1, stations_dev * local * 2 * points)


def traces_of(arrived, table, points):
    groups = arrived.shape[0]
    stations_dev = arrived.size // (groups * 128)
    local = 128 // (2 * points)
    spec = arrived.reshape(groups, stations_dev, local, 2, points)
    tab = table.reshape(groups, local, 2, table.shape[1])
    mixed = lax.dot_general(
        spec,
        tab,
        (((0, 2, 3), (0, 1, 2)), ((), ())),
        precision=lax.Precision.HIGHEST,
        preferred_element_type=jnp.float32,
    )
    scaled = mixed * (1.0 / math.sqrt(table.shape[0] // 2))
    return scaled.transpose(1, 0, 2)


def windowed(traces, onset_index):
    time_index = jnp.arange(traces.shape[2], dtype=jnp.int32)
    distance = jnp.abs(time_index - traces.shape[2] // 2)
    keep = distance[None, None, :] < onset_index[:, :, None]
    return jnp.where(keep, traces, jnp.zeros_like(traces))


def per_device(reflection, focus_plus, focus_direct, onset_index):
    groups = lax.axis_size("af")
    points = focus_plus.shape[0]
    table = base_table(NFREQ, NT)

    def convolve(spectra, product):
        arrived = lax.all_to_all(spectra, "af", 0, 0, tiled=True)
        stations = arrived.size // 128
        result = product(reflection, arrived.reshape(stations, 128))
        result = result.reshape(arrived.shape)
        return lax.all_to_all(result, "af", 0, 0, tiled=True)

    images = convolve(spectra_of(focus_plus, table, groups), forward_kernel)
    focus_minus = windowed(traces_of(images, table, points), onset_index)
    returns = convolve(spectra_of(focus_minus, table, groups), adjoint_kernel)
    focus_next = focus_direct + windowed(traces_of(returns, table, points), onset_index)
    return (focus_minus, focus_next)


def solution(mesh):
    return jax.shard_map(
        per_device,
        mesh=mesh,
        in_specs=(
            P(None, "af", None, None),
            P(None, "af", None),
            P(None, "af", None),
            P(None, "af"),
        ),
        out_specs=(P(None, "af", None), P(None, "af", None)),
        check_vma=False,
    )
```

```python
import math

import numpy as np

import jax
import jax.numpy as jnp
from jax import lax
from jax.experimental import pallas as pl
from jax.experimental.pallas import tpu as pltpu
from jax.sharding import PartitionSpec as P

NFREQ = 256
NT = 512
TS = 512


def _partner(x, negate_first):
    x = x.astype(jnp.float32)
    lane = lax.broadcasted_iota(jnp.int32, x.shape, 1)
    first = (lane % 64) < 32
    ahead = pltpu.roll(x, 96, 1)
    behind = pltpu.roll(x, 32, 1)
    if negate_first:
        out = jnp.where(first, -ahead, behind)
    else:
        out = jnp.where(first, ahead, -behind)
    return out.astype(jnp.bfloat16)


def _fwd_kernel(x_ref, r_ref, o_ref, xp_ref):
    @pl.when(pl.program_id(0) == 0)
    def _():
        xp_ref[...] = _partner(x_ref[...], True)

    parts = []
    for kl in range(2):
        x = x_ref[:, kl * 64:(kl + 1) * 64]
        xp = xp_ref[:, kl * 64:(kl + 1) * 64]
        a = jnp.dot(r_ref[0, kl], x, preferred_element_type=jnp.float32)
        a = a + jnp.dot(r_ref[1, kl], xp, preferred_element_type=jnp.float32)
        parts.append(a)
    o_ref[...] = jnp.concatenate(parts, 1)


def forward_kernel(reflection, x):
    stations = x.shape[0]
    return pl.pallas_call(
        _fwd_kernel,
        grid=(stations // TS,),
        in_specs=[
            pl.BlockSpec((stations, 128), lambda i: (0, 0)),
            pl.BlockSpec((2, 2, TS, stations), lambda i: (0, 0, i, 0)),
        ],
        out_specs=pl.BlockSpec((TS, 128), lambda i: (i, 0)),
        out_shape=jax.ShapeDtypeStruct((stations, 128), jnp.float32),
        scratch_shapes=[pltpu.VMEM((stations, 128), jnp.bfloat16)],
    )(x, reflection)


def _adj_kernel(y_ref, r_ref, o_ref, yp_ref, acc_ref):
    i = pl.program_id(0)

    @pl.when(i == 0)
    def _():
        yp_ref[...] = _partner(y_ref[...], False)
        acc_ref[...] = jnp.zeros(acc_ref.shape, jnp.float32)

    off = pl.multiple_of(i * TS, TS)
    y = y_ref[pl.ds(off, TS), :]
    yp = yp_ref[pl.ds(off, TS), :]
    dims = (((0,), (0,)), ((), ()))
    parts = []
    for kl in range(2):
        a = lax.dot_general(r_ref[0, kl], y[:, kl * 64:(kl + 1) * 64], dims,
                            preferred_element_type=jnp.float32)
        a = a + lax.dot_general(r_ref[1, kl], yp[:, kl * 64:(kl + 1) * 64], dims,
                                preferred_element_type=jnp.float32)
        parts.append(a)
    acc_ref[...] += jnp.concatenate(parts, 1)

    @pl.when(i == pl.num_programs(0) - 1)
    def _():
        o_ref[...] = acc_ref[...]


def adjoint_kernel(reflection, y):
    stations = y.shape[0]
    return pl.pallas_call(
        _adj_kernel,
        grid=(stations // TS,),
        in_specs=[
            pl.BlockSpec((stations, 128), lambda i: (0, 0)),
            pl.BlockSpec((2, 2, TS, stations), lambda i: (0, 0, i, 0)),
        ],
        out_specs=pl.BlockSpec((stations, 128), lambda i: (0, 0)),
        out_shape=jax.ShapeDtypeStruct((stations, 128), jnp.float32),
        scratch_shapes=[
            pltpu.VMEM((stations, 128), jnp.bfloat16),
            pltpu.VMEM((stations, 128), jnp.float32),
        ],
    )(y, reflection)


def base_table(nfreq, ntime):
    phase = (np.arange(nfreq)[:, None] * np.arange(ntime)[None, :]) % ntime
    angle = phase.astype(np.float64) * (2.0 * math.pi / ntime)
    table = np.stack([np.cos(angle), -np.sin(angle)], 1).reshape(2 * nfreq, ntime)
    return jnp.asarray(table.astype(np.float32))


def spectra_of(traces, table, groups):
    points, stations_dev, ntime = traces.shape
    mixed = lax.dot_general(
        traces,
        table,
        (((2,), (1,)), ((), ())),
        precision=lax.Precision.HIGHEST,
        preferred_element_type=jnp.float32,
    )
    scaled = (mixed * (1.0 / math.sqrt(ntime))).astype(jnp.bfloat16)
    local = table.shape[0] // 2 // groups
    scaled = scaled.reshape(points, stations_dev, groups, local, 2)
    scaled = scaled.transpose(2, 1, 3, 4, 0)
    return scaled.reshape(groups, stations_dev, local * 2 * points)


def traces_of(arrived, table, points):
    groups = arrived.shape[0]
    stations_dev = arrived.size // (groups * 128)
    local = 128 // (2 * points)
    spec = arrived.reshape(groups, stations_dev, local, 2, points)
    tab = table.reshape(groups, local, 2, table.shape[1])
    mixed = lax.dot_general(
        spec,
        tab,
        (((0, 2, 3), (0, 1, 2)), ((), ())),
        precision=lax.Precision.HIGHEST,
        preferred_element_type=jnp.float32,
    )
    scaled = mixed * (1.0 / math.sqrt(table.shape[0] // 2))
    return scaled.transpose(1, 0, 2)


def windowed(traces, onset_index):
    time_index = jnp.arange(traces.shape[2], dtype=jnp.int32)
    distance = jnp.abs(time_index - traces.shape[2] // 2)
    keep = distance[None, None, :] < onset_index[:, :, None]
    return jnp.where(keep, traces, jnp.zeros_like(traces))


def per_device(reflection, focus_plus, focus_direct, onset_index):
    groups = lax.axis_size("af")
    points = focus_plus.shape[0]
    table = base_table(NFREQ, NT)

    def convolve(spectra, product):
        arrived = lax.all_to_all(spectra, "af", 0, 0, tiled=True)
        stations = arrived.size // 128
        result = product(reflection, arrived.reshape(stations, 128))
        result = result.reshape(arrived.shape[0], 1, -1)
        return lax.all_to_all(result, "af", 0, 0, tiled=True)

    images = convolve(spectra_of(focus_plus, table, groups), forward_kernel)
    focus_minus = windowed(traces_of(images, table, points), onset_index)
    returns = convolve(spectra_of(focus_minus, table, groups), adjoint_kernel)
    focus_next = focus_direct + windowed(traces_of(returns, table, points), onset_index)
    return (focus_minus, focus_next)


def solution(mesh):
    return jax.shard_map(
        per_device,
        mesh=mesh,
        in_specs=(
            P(None, "af", None, None),
            P(None, "af", None),
            P(None, "af", None),
            P(None, "af"),
        ),
        out_specs=(P(None, "af", None), P(None, "af", None)),
        check_vma=False,
    )
```

```python
import math

import numpy as np

import jax
import jax.numpy as jnp
from jax import lax
from jax.experimental import pallas as pl
from jax.experimental.pallas import tpu as pltpu
from jax.sharding import PartitionSpec as P

NFREQ = 256
NT = 512
TS = 512


def _partner(x, negate_first):
    x = x.astype(jnp.float32)
    lane = lax.broadcasted_iota(jnp.int32, x.shape, 1)
    first = (lane % 64) < 32
    ahead = pltpu.roll(x, 96, 1)
    behind = pltpu.roll(x, 32, 1)
    if negate_first:
        out = jnp.where(first, -ahead, behind)
    else:
        out = jnp.where(first, ahead, -behind)
    return out.astype(jnp.bfloat16)


def _fwd_kernel(x_ref, r_ref, o_ref, xp_ref):
    @pl.when(pl.program_id(0) == 0)
    def _():
        xp_ref[...] = _partner(x_ref[...], True)

    parts = []
    for kl in range(2):
        x = x_ref[:, kl * 64:(kl + 1) * 64]
        xp = xp_ref[:, kl * 64:(kl + 1) * 64]
        a = jnp.dot(r_ref[0, kl], x, preferred_element_type=jnp.float32)
        a = a + jnp.dot(r_ref[1, kl], xp, preferred_element_type=jnp.float32)
        parts.append(a)
    o_ref[...] = jnp.concatenate(parts, 1)


def forward_kernel(reflection, x):
    stations = x.shape[0]
    return pl.pallas_call(
        _fwd_kernel,
        grid=(stations // TS,),
        in_specs=[
            pl.BlockSpec((stations, 128), lambda i: (0, 0)),
            pl.BlockSpec((2, 2, TS, stations), lambda i: (0, 0, i, 0)),
        ],
        out_specs=pl.BlockSpec((TS, 128), lambda i: (i, 0)),
        out_shape=jax.ShapeDtypeStruct((stations, 128), jnp.float32),
        scratch_shapes=[pltpu.VMEM((stations, 128), jnp.bfloat16)],
    )(x, reflection)


def _adj_kernel(y_ref, r_ref, o_ref, yp_ref, acc_ref):
    i = pl.program_id(0)

    @pl.when(i == 0)
    def _():
        yp_ref[...] = _partner(y_ref[...], False)
        acc_ref[...] = jnp.zeros(acc_ref.shape, jnp.float32)

    off = pl.multiple_of(i * TS, TS)
    y = y_ref[pl.ds(off, TS), :]
    yp = yp_ref[pl.ds(off, TS), :]
    dims = (((0,), (0,)), ((), ()))
    parts = []
    for kl in range(2):
        a = lax.dot_general(r_ref[0, kl], y[:, kl * 64:(kl + 1) * 64], dims,
                            preferred_element_type=jnp.float32)
        a = a + lax.dot_general(r_ref[1, kl], yp[:, kl * 64:(kl + 1) * 64], dims,
                                preferred_element_type=jnp.float32)
        parts.append(a)
    acc_ref[...] += jnp.concatenate(parts, 1)

    @pl.when(i == pl.num_programs(0) - 1)
    def _():
        o_ref[...] = acc_ref[...]


def adjoint_kernel(reflection, y):
    stations = y.shape[0]
    return pl.pallas_call(
        _adj_kernel,
        grid=(stations // TS,),
        in_specs=[
            pl.BlockSpec((stations, 128), lambda i: (0, 0)),
            pl.BlockSpec((2, 2, TS, stations), lambda i: (0, 0, i, 0)),
        ],
        out_specs=pl.BlockSpec((stations, 128), lambda i: (0, 0)),
        out_shape=jax.ShapeDtypeStruct((stations, 128), jnp.float32),
        scratch_shapes=[
            pltpu.VMEM((stations, 128), jnp.bfloat16),
            pltpu.VMEM((stations, 128), jnp.float32),
        ],
    )(y, reflection)


def base_table(nfreq, ntime):
    phase = (np.arange(nfreq)[:, None] * np.arange(ntime)[None, :]) % ntime
    angle = phase.astype(np.float64) * (2.0 * math.pi / ntime)
    table = np.stack([np.cos(angle), -np.sin(angle)], 1).reshape(2 * nfreq, ntime)
    return jnp.asarray(table.astype(np.float32))


def spectra_of(traces, table, groups):
    points, stations_dev, ntime = traces.shape
    tab = table.reshape(groups, table.shape[0] // groups, ntime)
    mixed = jnp.einsum("pst,dqt->dsqp", traces, tab,
        precision=lax.Precision.HIGHEST,
        preferred_element_type=jnp.float32,
    )
    scaled = (mixed * (1.0 / math.sqrt(ntime))).astype(jnp.bfloat16)
    return scaled.reshape(groups, stations_dev, tab.shape[1] * points)


def traces_of(arrived, table, points):
    groups = arrived.shape[0]
    stations_dev = arrived.size // (groups * 128)
    local = 128 // (2 * points)
    spec = arrived.reshape(groups, stations_dev, local, 2, points)
    tab = table.reshape(groups, local, 2, table.shape[1])
    mixed = lax.dot_general(
        spec,
        tab,
        (((0, 2, 3), (0, 1, 2)), ((), ())),
        precision=lax.Precision.HIGHEST,
        preferred_element_type=jnp.float32,
    )
    scaled = mixed * (1.0 / math.sqrt(table.shape[0] // 2))
    return scaled.transpose(1, 0, 2)


def windowed(traces, onset_index):
    time_index = jnp.arange(traces.shape[2], dtype=jnp.int32)
    distance = jnp.abs(time_index - traces.shape[2] // 2)
    keep = distance[None, None, :] < onset_index[:, :, None]
    return jnp.where(keep, traces, jnp.zeros_like(traces))


def per_device(reflection, focus_plus, focus_direct, onset_index):
    groups = lax.axis_size("af")
    points = focus_plus.shape[0]
    table = base_table(NFREQ, NT)

    def convolve(spectra, product):
        arrived = lax.all_to_all(spectra, "af", 0, 0, tiled=True)
        stations = arrived.size // 128
        result = product(reflection, arrived.reshape(stations, 128))
        result = result.reshape(arrived.shape[0], 1, -1)
        return lax.all_to_all(result, "af", 0, 0, tiled=True)

    images = convolve(spectra_of(focus_plus, table, groups), forward_kernel)
    focus_minus = windowed(traces_of(images, table, points), onset_index)
    returns = convolve(spectra_of(focus_minus, table, groups), adjoint_kernel)
    focus_next = focus_direct + windowed(traces_of(returns, table, points), onset_index)
    return (focus_minus, focus_next)


def solution(mesh):
    return jax.shard_map(
        per_device,
        mesh=mesh,
        in_specs=(
            P(None, "af", None, None),
            P(None, "af", None),
            P(None, "af", None),
            P(None, "af"),
        ),
        out_specs=(P(None, "af", None), P(None, "af", None)),
        check_vma=False,
    )
```

```python
import math

import numpy as np

import jax
import jax.numpy as jnp
from jax import lax
from jax.experimental import pallas as pl
from jax.experimental.pallas import tpu as pltpu
from jax.sharding import PartitionSpec as P

NFREQ = 256
NT = 512
TS = 512


def _partner(x, negate_first):
    x = x.astype(jnp.float32)
    lane = lax.broadcasted_iota(jnp.int32, x.shape, 1)
    first = (lane % 64) < 32
    ahead = pltpu.roll(x, 96, 1)
    behind = pltpu.roll(x, 32, 1)
    if negate_first:
        out = jnp.where(first, -ahead, behind)
    else:
        out = jnp.where(first, ahead, -behind)
    return out.astype(jnp.bfloat16)


def _fwd_kernel(x_ref, r_ref, o_ref, xp_ref):
    @pl.when(pl.program_id(0) == 0)
    def _():
        xp_ref[...] = _partner(x_ref[...], True)

    parts = []
    for kl in range(2):
        x = x_ref[:, kl * 64:(kl + 1) * 64]
        xp = xp_ref[:, kl * 64:(kl + 1) * 64]
        a = jnp.dot(r_ref[0, kl], x, preferred_element_type=jnp.float32)
        a = a + jnp.dot(r_ref[1, kl], xp, preferred_element_type=jnp.float32)
        parts.append(a)
    o_ref[...] = jnp.concatenate(parts, 1)


def forward_kernel(reflection, x):
    stations = x.shape[0]
    return pl.pallas_call(
        _fwd_kernel,
        grid=(stations // TS,),
        in_specs=[
            pl.BlockSpec((stations, 128), lambda i: (0, 0)),
            pl.BlockSpec((2, 2, TS, stations), lambda i: (0, 0, i, 0)),
        ],
        out_specs=pl.BlockSpec((TS, 128), lambda i: (i, 0)),
        out_shape=jax.ShapeDtypeStruct((stations, 128), jnp.float32),
        scratch_shapes=[pltpu.VMEM((stations, 128), jnp.bfloat16)],
    )(x, reflection)


def _adj_kernel(y_ref, r_ref, o_ref, yp_ref, acc_ref):
    i = pl.program_id(0)

    @pl.when(i == 0)
    def _():
        yp_ref[...] = _partner(y_ref[...], False)
        acc_ref[...] = jnp.zeros(acc_ref.shape, jnp.float32)

    off = pl.multiple_of(i * TS, TS)
    y = y_ref[pl.ds(off, TS), :]
    yp = yp_ref[pl.ds(off, TS), :]
    dims = (((0,), (0,)), ((), ()))
    parts = []
    for kl in range(2):
        a = lax.dot_general(r_ref[0, kl], y[:, kl * 64:(kl + 1) * 64], dims,
                            preferred_element_type=jnp.float32)
        a = a + lax.dot_general(r_ref[1, kl], yp[:, kl * 64:(kl + 1) * 64], dims,
                                preferred_element_type=jnp.float32)
        parts.append(a)
    acc_ref[...] += jnp.concatenate(parts, 1)

    @pl.when(i == pl.num_programs(0) - 1)
    def _():
        o_ref[...] = acc_ref[...]


def adjoint_kernel(reflection, y):
    stations = y.shape[0]
    return pl.pallas_call(
        _adj_kernel,
        grid=(stations // TS,),
        in_specs=[
            pl.BlockSpec((stations, 128), lambda i: (0, 0)),
            pl.BlockSpec((2, 2, TS, stations), lambda i: (0, 0, i, 0)),
        ],
        out_specs=pl.BlockSpec((stations, 128), lambda i: (0, 0)),
        out_shape=jax.ShapeDtypeStruct((stations, 128), jnp.float32),
        scratch_shapes=[
            pltpu.VMEM((stations, 128), jnp.bfloat16),
            pltpu.VMEM((stations, 128), jnp.float32),
        ],
    )(y, reflection)


def base_table(nfreq, ntime):
    freq_index = jnp.arange(nfreq, dtype=jnp.int32)
    time_index = jnp.arange(ntime, dtype=jnp.int32)
    phase = freq_index[:, None] * time_index[None, :] % ntime
    angle = phase.astype(jnp.float32) * (2.0 * math.pi / ntime)
    return jnp.stack([jnp.cos(angle), -jnp.sin(angle)], 1).reshape(2 * nfreq, ntime)


def spectra_of(traces, table, groups):
    points, stations_dev, ntime = traces.shape
    tab = table.reshape(groups, table.shape[0] // groups, ntime)
    mixed = jnp.einsum("pst,dqt->dsqp", traces, tab,
        precision=lax.Precision.HIGHEST,
        preferred_element_type=jnp.float32,
    )
    scaled = (mixed * (1.0 / math.sqrt(ntime))).astype(jnp.bfloat16)
    return scaled.reshape(groups, stations_dev, tab.shape[1] * points)


def traces_of(arrived, table, points):
    groups = arrived.shape[0]
    stations_dev = arrived.size // (groups * 128)
    local = 128 // (2 * points)
    spec = arrived.reshape(groups, stations_dev, local, 2, points)
    tab = table.reshape(groups, local, 2, table.shape[1])
    mixed = lax.dot_general(
        spec,
        tab,
        (((0, 2, 3), (0, 1, 2)), ((), ())),
        precision=lax.Precision.HIGHEST,
        preferred_element_type=jnp.float32,
    )
    scaled = mixed * (1.0 / math.sqrt(table.shape[0] // 2))
    return scaled.transpose(1, 0, 2)


def windowed(traces, onset_index):
    time_index = jnp.arange(traces.shape[2], dtype=jnp.int32)
    distance = jnp.abs(time_index - traces.shape[2] // 2)
    keep = distance[None, None, :] < onset_index[:, :, None]
    return jnp.where(keep, traces, jnp.zeros_like(traces))


def per_device(reflection, focus_plus, focus_direct, onset_index):
    groups = lax.axis_size("af")
    points = focus_plus.shape[0]
    table = base_table(NFREQ, NT)

    def convolve(spectra, product):
        arrived = lax.all_to_all(spectra, "af", 0, 0, tiled=True)
        stations = arrived.size // 128
        result = product(reflection, arrived.reshape(stations, 128))
        result = result.reshape(arrived.shape[0], 1, -1)
        return lax.all_to_all(result, "af", 0, 0, tiled=True)

    images = convolve(spectra_of(focus_plus, table, groups), forward_kernel)
    focus_minus = windowed(traces_of(images, table, points), onset_index)
    returns = convolve(spectra_of(focus_minus, table, groups), adjoint_kernel)
    focus_next = focus_direct + windowed(traces_of(returns, table, points), onset_index)
    return (focus_minus, focus_next)


def solution(mesh):
    return jax.shard_map(
        per_device,
        mesh=mesh,
        in_specs=(
            P(None, "af", None, None),
            P(None, "af", None),
            P(None, "af", None),
            P(None, "af"),
        ),
        out_specs=(P(None, "af", None), P(None, "af", None)),
        check_vma=False,
    )
```

```python
import math

import numpy as np

import jax
import jax.numpy as jnp
from jax import lax
from jax.experimental import pallas as pl
from jax.experimental.pallas import tpu as pltpu
from jax.sharding import PartitionSpec as P

NFREQ = 256
NT = 512
TS = 512


def _partner(x, negate_first):
    x = x.astype(jnp.float32)
    lane = lax.broadcasted_iota(jnp.int32, x.shape, 1)
    first = (lane % 64) < 32
    ahead = pltpu.roll(x, 96, 1)
    behind = pltpu.roll(x, 32, 1)
    if negate_first:
        out = jnp.where(first, -ahead, behind)
    else:
        out = jnp.where(first, ahead, -behind)
    return out.astype(jnp.bfloat16)


def _fwd_kernel(x_ref, r_ref, o_ref, xp_ref):
    @pl.when(pl.program_id(0) == 0)
    def _():
        xp_ref[...] = _partner(x_ref[...], True)

    parts = []
    for kl in range(2):
        x = x_ref[:, kl * 64:(kl + 1) * 64]
        xp = xp_ref[:, kl * 64:(kl + 1) * 64]
        a = jnp.dot(r_ref[0, kl], x, preferred_element_type=jnp.float32)
        a = a + jnp.dot(r_ref[1, kl], xp, preferred_element_type=jnp.float32)
        parts.append(a)
    o_ref[...] = jnp.concatenate(parts, 1)


def forward_kernel(reflection, x):
    stations = x.shape[0]
    return pl.pallas_call(
        _fwd_kernel,
        grid=(stations // TS,),
        in_specs=[
            pl.BlockSpec((stations, 128), lambda i: (0, 0)),
            pl.BlockSpec((2, 2, TS, stations), lambda i: (0, 0, i, 0)),
        ],
        out_specs=pl.BlockSpec((TS, 128), lambda i: (i, 0)),
        out_shape=jax.ShapeDtypeStruct((stations, 128), jnp.float32),
        scratch_shapes=[pltpu.VMEM((stations, 128), jnp.bfloat16)],
    )(x, reflection)


def _adj_kernel(y_ref, r_ref, o_ref, yp_ref, acc_ref):
    i = pl.program_id(0)

    @pl.when(i == 0)
    def _():
        yp_ref[...] = _partner(y_ref[...], False)
        acc_ref[...] = jnp.zeros(acc_ref.shape, jnp.float32)

    off = pl.multiple_of(i * TS, TS)
    y = y_ref[pl.ds(off, TS), :]
    yp = yp_ref[pl.ds(off, TS), :]
    dims = (((0,), (0,)), ((), ()))
    parts = []
    for kl in range(2):
        a = lax.dot_general(r_ref[0, kl], y[:, kl * 64:(kl + 1) * 64], dims,
                            preferred_element_type=jnp.float32)
        a = a + lax.dot_general(r_ref[1, kl], yp[:, kl * 64:(kl + 1) * 64], dims,
                                preferred_element_type=jnp.float32)
        parts.append(a)
    acc_ref[...] += jnp.concatenate(parts, 1)

    @pl.when(i == pl.num_programs(0) - 1)
    def _():
        o_ref[...] = acc_ref[...]


def adjoint_kernel(reflection, y):
    stations = y.shape[0]
    return pl.pallas_call(
        _adj_kernel,
        grid=(stations // TS,),
        in_specs=[
            pl.BlockSpec((stations, 128), lambda i: (0, 0)),
            pl.BlockSpec((2, 2, TS, stations), lambda i: (0, 0, i, 0)),
        ],
        out_specs=pl.BlockSpec((stations, 128), lambda i: (0, 0)),
        out_shape=jax.ShapeDtypeStruct((stations, 128), jnp.float32),
        scratch_shapes=[
            pltpu.VMEM((stations, 128), jnp.bfloat16),
            pltpu.VMEM((stations, 128), jnp.float32),
        ],
    )(y, reflection)


def base_table(nfreq, ntime):
    phase = (np.arange(nfreq)[:, None] * np.arange(ntime)[None, :]) % ntime
    angle = phase.astype(np.float64) * (2.0 * math.pi / ntime)
    table = np.stack([np.cos(angle), -np.sin(angle)], 1).reshape(2 * nfreq, ntime)
    return jnp.asarray(table.astype(np.float32))


def spectra_of(traces, table, groups):
    points, stations_dev, ntime = traces.shape
    tab = table.reshape(groups, table.shape[0] // groups, ntime)
    mixed = jnp.einsum("pst,dqt->dsqp", traces, tab,
        precision=lax.Precision.HIGH,
        preferred_element_type=jnp.float32,
    )
    scaled = (mixed * (1.0 / math.sqrt(ntime))).astype(jnp.bfloat16)
    return scaled.reshape(groups, stations_dev, tab.shape[1] * points)


def traces_of(arrived, table, points):
    groups = arrived.shape[0]
    stations_dev = arrived.size // (groups * 128)
    local = 128 // (2 * points)
    spec = arrived.reshape(groups, stations_dev, local, 2, points)
    tab = table.reshape(groups, local, 2, table.shape[1])
    mixed = lax.dot_general(
        spec,
        tab,
        (((0, 2, 3), (0, 1, 2)), ((), ())),
        precision=lax.Precision.HIGH,
        preferred_element_type=jnp.float32,
    )
    scaled = mixed * (1.0 / math.sqrt(table.shape[0] // 2))
    return scaled.transpose(1, 0, 2)


def windowed(traces, onset_index):
    time_index = jnp.arange(traces.shape[2], dtype=jnp.int32)
    distance = jnp.abs(time_index - traces.shape[2] // 2)
    keep = distance[None, None, :] < onset_index[:, :, None]
    return jnp.where(keep, traces, jnp.zeros_like(traces))


def per_device(reflection, focus_plus, focus_direct, onset_index):
    groups = lax.axis_size("af")
    points = focus_plus.shape[0]
    table = base_table(NFREQ, NT)

    def convolve(spectra, product):
        arrived = lax.all_to_all(spectra, "af", 0, 0, tiled=True)
        stations = arrived.size // 128
        result = product(reflection, arrived.reshape(stations, 128))
        result = result.reshape(arrived.shape[0], 1, -1)
        return lax.all_to_all(result, "af", 0, 0, tiled=True)

    images = convolve(spectra_of(focus_plus, table, groups), forward_kernel)
    focus_minus = windowed(traces_of(images, table, points), onset_index)
    returns = convolve(spectra_of(focus_minus, table, groups), adjoint_kernel)
    focus_next = focus_direct + windowed(traces_of(returns, table, points), onset_index)
    return (focus_minus, focus_next)


def solution(mesh):
    return jax.shard_map(
        per_device,
        mesh=mesh,
        in_specs=(
            P(None, "af", None, None),
            P(None, "af", None),
            P(None, "af", None),
            P(None, "af"),
        ),
        out_specs=(P(None, "af", None), P(None, "af", None)),
        check_vma=False,
    )
```

```python
import math

import numpy as np

import jax
import jax.numpy as jnp
from jax import lax
from jax.experimental import pallas as pl
from jax.experimental.pallas import tpu as pltpu
from jax.sharding import PartitionSpec as P

NFREQ = 256
NT = 512
TS = 512
TS_ADJ = 768


def _partner(x, negate_first):
    x = x.astype(jnp.float32)
    lane = lax.broadcasted_iota(jnp.int32, x.shape, 1)
    first = (lane % 64) < 32
    ahead = pltpu.roll(x, 96, 1)
    behind = pltpu.roll(x, 32, 1)
    if negate_first:
        out = jnp.where(first, -ahead, behind)
    else:
        out = jnp.where(first, ahead, -behind)
    return out.astype(jnp.bfloat16)


def _fwd_kernel(x_ref, r_ref, o_ref, xp_ref):
    @pl.when(pl.program_id(0) == 0)
    def _():
        xp_ref[...] = _partner(x_ref[...], True)

    parts = []
    for kl in range(2):
        x = x_ref[:, kl * 64:(kl + 1) * 64]
        xp = xp_ref[:, kl * 64:(kl + 1) * 64]
        a = jnp.dot(r_ref[0, kl], x, preferred_element_type=jnp.float32)
        a = a + jnp.dot(r_ref[1, kl], xp, preferred_element_type=jnp.float32)
        parts.append(a)
    o_ref[...] = jnp.concatenate(parts, 1)


def forward_kernel(reflection, x):
    stations = x.shape[0]
    return pl.pallas_call(
        _fwd_kernel,
        grid=(stations // TS,),
        in_specs=[
            pl.BlockSpec((stations, 128), lambda i: (0, 0)),
            pl.BlockSpec((2, 2, TS, stations), lambda i: (0, 0, i, 0)),
        ],
        out_specs=pl.BlockSpec((TS, 128), lambda i: (i, 0)),
        out_shape=jax.ShapeDtypeStruct((stations, 128), jnp.float32),
        scratch_shapes=[pltpu.VMEM((stations, 128), jnp.bfloat16)],
    )(x, reflection)


def _adj_kernel(y_ref, r_ref, o_ref, yp_ref, acc_ref):
    i = pl.program_id(0)

    @pl.when(i == 0)
    def _():
        yp_ref[...] = _partner(y_ref[...], False)
        acc_ref[...] = jnp.zeros(acc_ref.shape, jnp.float32)

    off = pl.multiple_of(i * TS_ADJ, TS_ADJ)
    y = y_ref[pl.ds(off, TS_ADJ), :]
    yp = yp_ref[pl.ds(off, TS_ADJ), :]
    dims = (((0,), (0,)), ((), ()))
    parts = []
    for kl in range(2):
        a = lax.dot_general(r_ref[0, kl], y[:, kl * 64:(kl + 1) * 64], dims,
                            preferred_element_type=jnp.float32)
        a = a + lax.dot_general(r_ref[1, kl], yp[:, kl * 64:(kl + 1) * 64], dims,
                                preferred_element_type=jnp.float32)
        parts.append(a)
    acc_ref[...] += jnp.concatenate(parts, 1)

    @pl.when(i == pl.num_programs(0) - 1)
    def _():
        o_ref[...] = acc_ref[...]


def adjoint_kernel(reflection, y):
    stations = y.shape[0]
    return pl.pallas_call(
        _adj_kernel,
        grid=(stations // TS_ADJ,),
        in_specs=[
            pl.BlockSpec((stations, 128), lambda i: (0, 0)),
            pl.BlockSpec((2, 2, TS_ADJ, stations), lambda i: (0, 0, i, 0)),
        ],
        out_specs=pl.BlockSpec((stations, 128), lambda i: (0, 0)),
        out_shape=jax.ShapeDtypeStruct((stations, 128), jnp.float32),
        scratch_shapes=[
            pltpu.VMEM((stations, 128), jnp.bfloat16),
            pltpu.VMEM((stations, 128), jnp.float32),
        ],
    )(y, reflection)


def base_table(nfreq, ntime):
    phase = (np.arange(nfreq)[:, None] * np.arange(ntime)[None, :]) % ntime
    angle = phase.astype(np.float64) * (2.0 * math.pi / ntime)
    table = np.stack([np.cos(angle), -np.sin(angle)], 1).reshape(2 * nfreq, ntime)
    return jnp.asarray(table.astype(np.float32))


def spectra_of(traces, table, groups):
    points, stations_dev, ntime = traces.shape
    tab = table.reshape(groups, table.shape[0] // groups, ntime)
    mixed = jnp.einsum("pst,dqt->dsqp", traces, tab,
        precision=lax.Precision.HIGH,
        preferred_element_type=jnp.float32,
    )
    scaled = (mixed * (1.0 / math.sqrt(ntime))).astype(jnp.bfloat16)
    return scaled.reshape(groups, stations_dev, tab.shape[1] * points)


def traces_of(arrived, table, points):
    groups = arrived.shape[0]
    stations_dev = arrived.size // (groups * 128)
    local = 128 // (2 * points)
    spec = arrived.reshape(groups, stations_dev, local, 2, points)
    tab = table.reshape(groups, local, 2, table.shape[1])
    mixed = lax.dot_general(
        spec,
        tab,
        (((0, 2, 3), (0, 1, 2)), ((), ())),
        precision=lax.Precision.HIGH,
        preferred_element_type=jnp.float32,
    )
    scaled = mixed * (1.0 / math.sqrt(table.shape[0] // 2))
    return scaled.transpose(1, 0, 2)


def windowed(traces, onset_index):
    time_index = jnp.arange(traces.shape[2], dtype=jnp.int32)
    distance = jnp.abs(time_index - traces.shape[2] // 2)
    keep = distance[None, None, :] < onset_index[:, :, None]
    return jnp.where(keep, traces, jnp.zeros_like(traces))


def per_device(reflection, focus_plus, focus_direct, onset_index):
    groups = lax.axis_size("af")
    points = focus_plus.shape[0]
    table = base_table(NFREQ, NT)

    def convolve(spectra, product):
        arrived = lax.all_to_all(spectra, "af", 0, 0, tiled=True)
        stations = arrived.size // 128
        result = product(reflection, arrived.reshape(stations, 128))
        result = result.reshape(arrived.shape[0], 1, -1)
        return lax.all_to_all(result, "af", 0, 0, tiled=True)

    images = convolve(spectra_of(focus_plus, table, groups), forward_kernel)
    focus_minus = windowed(traces_of(images, table, points), onset_index)
    returns = convolve(spectra_of(focus_minus, table, groups), adjoint_kernel)
    focus_next = focus_direct + windowed(traces_of(returns, table, points), onset_index)
    return (focus_minus, focus_next)


def solution(mesh):
    return jax.shard_map(
        per_device,
        mesh=mesh,
        in_specs=(
            P(None, "af", None, None),
            P(None, "af", None),
            P(None, "af", None),
            P(None, "af"),
        ),
        out_specs=(P(None, "af", None), P(None, "af", None)),
        check_vma=False,
    )
```

```python
import math

import numpy as np

import jax
import jax.numpy as jnp
from jax import lax
from jax.experimental import pallas as pl
from jax.experimental.pallas import tpu as pltpu
from jax.sharding import PartitionSpec as P

NFREQ = 256
NT = 512
TS = 512


def _partner(x, negate_first):
    x = x.astype(jnp.float32)
    lane = lax.broadcasted_iota(jnp.int32, x.shape, 1)
    first = (lane % 64) < 32
    ahead = pltpu.roll(x, 96, 1)
    behind = pltpu.roll(x, 32, 1)
    if negate_first:
        out = jnp.where(first, -ahead, behind)
    else:
        out = jnp.where(first, ahead, -behind)
    return out.astype(jnp.bfloat16)


def _gather(src_hbm, dst_ref, sems):
    groups, rows = src_hbm.shape[0], src_hbm.shape[1]
    copies = [
        pltpu.make_async_copy(src_hbm.at[j], dst_ref.at[pl.ds(j * rows, rows)], sems.at[j])
        for j in range(groups)
    ]
    for c in copies:
        c.start()
    for c in copies:
        c.wait()


def _fwd_kernel(xa_hbm, r_ref, o_ref, x_ref, xp_ref, sems):
    @pl.when(pl.program_id(0) == 0)
    def _():
        _gather(xa_hbm, x_ref, sems)
        xp_ref[...] = _partner(x_ref[...], True)

    parts = []
    for kl in range(2):
        x = x_ref[:, kl * 64:(kl + 1) * 64]
        xp = xp_ref[:, kl * 64:(kl + 1) * 64]
        a = jnp.dot(r_ref[0, kl], x, preferred_element_type=jnp.float32)
        a = a + jnp.dot(r_ref[1, kl], xp, preferred_element_type=jnp.float32)
        parts.append(a)
    o_ref[...] = jnp.concatenate(parts, 1)


def forward_kernel(reflection, x):
    stations = x.shape[0] * x.shape[1]
    return pl.pallas_call(
        _fwd_kernel,
        grid=(stations // TS,),
        in_specs=[
            pl.BlockSpec(memory_space=pl.ANY),
            pl.BlockSpec((2, 2, TS, stations), lambda i: (0, 0, i, 0)),
        ],
        out_specs=pl.BlockSpec((TS, 128), lambda i: (i, 0)),
        out_shape=jax.ShapeDtypeStruct((stations, 128), jnp.float32),
        scratch_shapes=[
            pltpu.VMEM((stations, 128), jnp.bfloat16),
            pltpu.VMEM((stations, 128), jnp.bfloat16),
            pltpu.SemaphoreType.DMA((x.shape[0],)),
        ],
    )(x, reflection)


def _adj_kernel(ya_hbm, r_ref, o_ref, y_ref, yp_ref, acc_ref, sems):
    i = pl.program_id(0)

    @pl.when(i == 0)
    def _():
        _gather(ya_hbm, y_ref, sems)
        yp_ref[...] = _partner(y_ref[...], False)
        acc_ref[...] = jnp.zeros(acc_ref.shape, jnp.float32)

    off = pl.multiple_of(i * TS, TS)
    y = y_ref[pl.ds(off, TS), :]
    yp = yp_ref[pl.ds(off, TS), :]
    dims = (((0,), (0,)), ((), ()))
    parts = []
    for kl in range(2):
        a = lax.dot_general(r_ref[0, kl], y[:, kl * 64:(kl + 1) * 64], dims,
                            preferred_element_type=jnp.float32)
        a = a + lax.dot_general(r_ref[1, kl], yp[:, kl * 64:(kl + 1) * 64], dims,
                                preferred_element_type=jnp.float32)
        parts.append(a)
    acc_ref[...] += jnp.concatenate(parts, 1)

    @pl.when(i == pl.num_programs(0) - 1)
    def _():
        o_ref[...] = acc_ref[...]


def adjoint_kernel(reflection, y):
    stations = y.shape[0] * y.shape[1]
    return pl.pallas_call(
        _adj_kernel,
        grid=(stations // TS,),
        in_specs=[
            pl.BlockSpec(memory_space=pl.ANY),
            pl.BlockSpec((2, 2, TS, stations), lambda i: (0, 0, i, 0)),
        ],
        out_specs=pl.BlockSpec((stations, 128), lambda i: (0, 0)),
        out_shape=jax.ShapeDtypeStruct((stations, 128), jnp.float32),
        scratch_shapes=[
            pltpu.VMEM((stations, 128), jnp.bfloat16),
            pltpu.VMEM((stations, 128), jnp.bfloat16),
            pltpu.VMEM((stations, 128), jnp.float32),
            pltpu.SemaphoreType.DMA((y.shape[0],)),
        ],
    )(y, reflection)


def base_table(nfreq, ntime):
    phase = (np.arange(nfreq)[:, None] * np.arange(ntime)[None, :]) % ntime
    angle = phase.astype(np.float64) * (2.0 * math.pi / ntime)
    table = np.stack([np.cos(angle), -np.sin(angle)], 1).reshape(2 * nfreq, ntime)
    return jnp.asarray(table.astype(np.float32))


def spectra_of(traces, table, groups):
    points, stations_dev, ntime = traces.shape
    tab = table.reshape(groups, table.shape[0] // groups, ntime)
    mixed = jnp.einsum("pst,dqt->dsqp", traces, tab,
        precision=lax.Precision.HIGH,
        preferred_element_type=jnp.float32,
    )
    scaled = (mixed * (1.0 / math.sqrt(ntime))).astype(jnp.bfloat16)
    return scaled.reshape(groups, stations_dev, tab.shape[1] * points)


def traces_of(arrived, table, points):
    groups = arrived.shape[0]
    stations_dev = arrived.size // (groups * 128)
    local = 128 // (2 * points)
    spec = arrived.reshape(groups, stations_dev, local, 2, points)
    tab = table.reshape(groups, local, 2, table.shape[1])
    mixed = lax.dot_general(
        spec,
        tab,
        (((0, 2, 3), (0, 1, 2)), ((), ())),
        precision=lax.Precision.HIGH,
        preferred_element_type=jnp.float32,
    )
    scaled = mixed * (1.0 / math.sqrt(table.shape[0] // 2))
    return scaled.transpose(1, 0, 2)


def windowed(traces, onset_index):
    time_index = jnp.arange(traces.shape[2], dtype=jnp.int32)
    distance = jnp.abs(time_index - traces.shape[2] // 2)
    keep = distance[None, None, :] < onset_index[:, :, None]
    return jnp.where(keep, traces, jnp.zeros_like(traces))


def per_device(reflection, focus_plus, focus_direct, onset_index):
    groups = lax.axis_size("af")
    points = focus_plus.shape[0]
    table = base_table(NFREQ, NT)

    def convolve(spectra, product):
        arrived = lax.all_to_all(spectra, "af", 0, 0, tiled=True)
        result = product(reflection, arrived)
        result = result.reshape(arrived.shape[0], 1, -1)
        return lax.all_to_all(result, "af", 0, 0, tiled=True)

    images = convolve(spectra_of(focus_plus, table, groups), forward_kernel)
    focus_minus = windowed(traces_of(images, table, points), onset_index)
    returns = convolve(spectra_of(focus_minus, table, groups), adjoint_kernel)
    focus_next = focus_direct + windowed(traces_of(returns, table, points), onset_index)
    return (focus_minus, focus_next)


def solution(mesh):
    return jax.shard_map(
        per_device,
        mesh=mesh,
        in_specs=(
            P(None, "af", None, None),
            P(None, "af", None),
            P(None, "af", None),
            P(None, "af"),
        ),
        out_specs=(P(None, "af", None), P(None, "af", None)),
        check_vma=False,
    )
```

```python
import math

import numpy as np

import jax
import jax.numpy as jnp
from jax import lax
from jax.experimental import pallas as pl
from jax.experimental.pallas import tpu as pltpu
from jax.sharding import PartitionSpec as P

NFREQ = 256
NT = 512
TS = 256
TS_ADJ = 512


def _partner(x, negate_first):
    x = x.astype(jnp.float32)
    lane = lax.broadcasted_iota(jnp.int32, x.shape, 1)
    first = (lane % 64) < 32
    ahead = pltpu.roll(x, 96, 1)
    behind = pltpu.roll(x, 32, 1)
    if negate_first:
        out = jnp.where(first, -ahead, behind)
    else:
        out = jnp.where(first, ahead, -behind)
    return out.astype(jnp.bfloat16)


def _fwd_kernel(x_ref, r_ref, o_ref, xp_ref):
    @pl.when(pl.program_id(0) == 0)
    def _():
        xp_ref[...] = _partner(x_ref[...], True)

    parts = []
    for kl in range(2):
        x = x_ref[:, kl * 64:(kl + 1) * 64]
        xp = xp_ref[:, kl * 64:(kl + 1) * 64]
        a = jnp.dot(r_ref[0, kl], x, preferred_element_type=jnp.float32)
        a = a + jnp.dot(r_ref[1, kl], xp, preferred_element_type=jnp.float32)
        parts.append(a)
    o_ref[...] = jnp.concatenate(parts, 1)


def forward_kernel(reflection, x):
    stations = x.shape[0]
    return pl.pallas_call(
        _fwd_kernel,
        grid=(stations // TS,),
        in_specs=[
            pl.BlockSpec((stations, 128), lambda i: (0, 0)),
            pl.BlockSpec((2, 2, TS, stations), lambda i: (0, 0, i, 0)),
        ],
        out_specs=pl.BlockSpec((TS, 128), lambda i: (i, 0)),
        out_shape=jax.ShapeDtypeStruct((stations, 128), jnp.float32),
        scratch_shapes=[pltpu.VMEM((stations, 128), jnp.bfloat16)],
    )(x, reflection)


def _adj_kernel(y_ref, r_ref, o_ref, yp_ref, acc_ref):
    i = pl.program_id(0)

    @pl.when(i == 0)
    def _():
        yp_ref[...] = _partner(y_ref[...], False)
        acc_ref[...] = jnp.zeros(acc_ref.shape, jnp.float32)

    off = pl.multiple_of(i * TS_ADJ, TS_ADJ)
    y = y_ref[pl.ds(off, TS_ADJ), :]
    yp = yp_ref[pl.ds(off, TS_ADJ), :]
    dims = (((0,), (0,)), ((), ()))
    parts = []
    for kl in range(2):
        a = lax.dot_general(r_ref[0, kl], y[:, kl * 64:(kl + 1) * 64], dims,
                            preferred_element_type=jnp.float32)
        a = a + lax.dot_general(r_ref[1, kl], yp[:, kl * 64:(kl + 1) * 64], dims,
                                preferred_element_type=jnp.float32)
        parts.append(a)
    acc_ref[...] += jnp.concatenate(parts, 1)

    @pl.when(i == pl.num_programs(0) - 1)
    def _():
        o_ref[...] = acc_ref[...]


def adjoint_kernel(reflection, y):
    stations = y.shape[0]
    return pl.pallas_call(
        _adj_kernel,
        grid=(stations // TS_ADJ,),
        in_specs=[
            pl.BlockSpec((stations, 128), lambda i: (0, 0)),
            pl.BlockSpec((2, 2, TS_ADJ, stations), lambda i: (0, 0, i, 0)),
        ],
        out_specs=pl.BlockSpec((stations, 128), lambda i: (0, 0)),
        out_shape=jax.ShapeDtypeStruct((stations, 128), jnp.float32),
        scratch_shapes=[
            pltpu.VMEM((stations, 128), jnp.bfloat16),
            pltpu.VMEM((stations, 128), jnp.float32),
        ],
    )(y, reflection)


def base_table(nfreq, ntime):
    phase = (np.arange(nfreq)[:, None] * np.arange(ntime)[None, :]) % ntime
    angle = phase.astype(np.float64) * (2.0 * math.pi / ntime)
    table = np.stack([np.cos(angle), -np.sin(angle)], 1).reshape(2 * nfreq, ntime)
    return jnp.asarray(table.astype(np.float32))


def spectra_of(traces, table, groups):
    points, stations_dev, ntime = traces.shape
    tab = table.reshape(groups, table.shape[0] // groups, ntime)
    mixed = jnp.einsum("pst,dqt->dsqp", traces, tab,
        precision=lax.Precision.HIGH,
        preferred_element_type=jnp.float32,
    )
    scaled = (mixed * (1.0 / math.sqrt(ntime))).astype(jnp.bfloat16)
    return scaled.reshape(groups, stations_dev, tab.shape[1] * points)


def traces_of(arrived, table, points):
    groups = arrived.shape[0]
    stations_dev = arrived.size // (groups * 128)
    local = 128 // (2 * points)
    spec = arrived.reshape(groups, stations_dev, local, 2, points)
    tab = table.reshape(groups, local, 2, table.shape[1])
    mixed = lax.dot_general(
        spec,
        tab,
        (((0, 2, 3), (0, 1, 2)), ((), ())),
        precision=lax.Precision.HIGH,
        preferred_element_type=jnp.float32,
    )
    scaled = mixed * (1.0 / math.sqrt(table.shape[0] // 2))
    return scaled.transpose(1, 0, 2)


def windowed(traces, onset_index):
    time_index = jnp.arange(traces.shape[2], dtype=jnp.int32)
    distance = jnp.abs(time_index - traces.shape[2] // 2)
    keep = distance[None, None, :] < onset_index[:, :, None]
    return jnp.where(keep, traces, jnp.zeros_like(traces))


def per_device(reflection, focus_plus, focus_direct, onset_index):
    groups = lax.axis_size("af")
    points = focus_plus.shape[0]
    table = base_table(NFREQ, NT)

    def convolve(spectra, product):
        arrived = lax.all_to_all(spectra, "af", 0, 0, tiled=True)
        stations = arrived.size // 128
        result = product(reflection, arrived.reshape(stations, 128))
        result = result.reshape(arrived.shape[0], 1, -1)
        return lax.all_to_all(result, "af", 0, 0, tiled=True)

    images = convolve(spectra_of(focus_plus, table, groups), forward_kernel)
    focus_minus = windowed(traces_of(images, table, points), onset_index)
    returns = convolve(spectra_of(focus_minus, table, groups), adjoint_kernel)
    focus_next = focus_direct + windowed(traces_of(returns, table, points), onset_index)
    return (focus_minus, focus_next)


def solution(mesh):
    return jax.shard_map(
        per_device,
        mesh=mesh,
        in_specs=(
            P(None, "af", None, None),
            P(None, "af", None),
            P(None, "af", None),
            P(None, "af"),
        ),
        out_specs=(P(None, "af", None), P(None, "af", None)),
        check_vma=False,
    )
```

```python
import math

import numpy as np

import jax
import jax.numpy as jnp
from jax import lax
from jax.experimental import pallas as pl
from jax.experimental.pallas import tpu as pltpu
from jax.sharding import PartitionSpec as P

NFREQ = 256
NT = 512
TS = 768
TS_ADJ = 512


def _partner(x, negate_first):
    x = x.astype(jnp.float32)
    lane = lax.broadcasted_iota(jnp.int32, x.shape, 1)
    first = (lane % 64) < 32
    ahead = pltpu.roll(x, 96, 1)
    behind = pltpu.roll(x, 32, 1)
    if negate_first:
        out = jnp.where(first, -ahead, behind)
    else:
        out = jnp.where(first, ahead, -behind)
    return out.astype(jnp.bfloat16)


def _fwd_kernel(x_ref, r_ref, o_ref, xp_ref):
    @pl.when(pl.program_id(0) == 0)
    def _():
        xp_ref[...] = _partner(x_ref[...], True)

    parts = []
    for kl in range(2):
        x = x_ref[:, kl * 64:(kl + 1) * 64]
        xp = xp_ref[:, kl * 64:(kl + 1) * 64]
        a = jnp.dot(r_ref[0, kl], x, preferred_element_type=jnp.float32)
        a = a + jnp.dot(r_ref[1, kl], xp, preferred_element_type=jnp.float32)
        parts.append(a)
    o_ref[...] = jnp.concatenate(parts, 1)


def forward_kernel(reflection, x):
    stations = x.shape[0]
    return pl.pallas_call(
        _fwd_kernel,
        grid=(stations // TS,),
        in_specs=[
            pl.BlockSpec((stations, 128), lambda i: (0, 0)),
            pl.BlockSpec((2, 2, TS, stations), lambda i: (0, 0, i, 0)),
        ],
        out_specs=pl.BlockSpec((TS, 128), lambda i: (i, 0)),
        out_shape=jax.ShapeDtypeStruct((stations, 128), jnp.float32),
        scratch_shapes=[pltpu.VMEM((stations, 128), jnp.bfloat16)],
    )(x, reflection)


def _adj_kernel(y_ref, r_ref, o_ref, yp_ref, acc_ref):
    i = pl.program_id(0)

    @pl.when(i == 0)
    def _():
        yp_ref[...] = _partner(y_ref[...], False)
        acc_ref[...] = jnp.zeros(acc_ref.shape, jnp.float32)

    off = pl.multiple_of(i * TS_ADJ, TS_ADJ)
    y = y_ref[pl.ds(off, TS_ADJ), :]
    yp = yp_ref[pl.ds(off, TS_ADJ), :]
    dims = (((0,), (0,)), ((), ()))
    parts = []
    for kl in range(2):
        a = lax.dot_general(r_ref[0, kl], y[:, kl * 64:(kl + 1) * 64], dims,
                            preferred_element_type=jnp.float32)
        a = a + lax.dot_general(r_ref[1, kl], yp[:, kl * 64:(kl + 1) * 64], dims,
                                preferred_element_type=jnp.float32)
        parts.append(a)
    acc_ref[...] += jnp.concatenate(parts, 1)

    @pl.when(i == pl.num_programs(0) - 1)
    def _():
        o_ref[...] = acc_ref[...]


def adjoint_kernel(reflection, y):
    stations = y.shape[0]
    return pl.pallas_call(
        _adj_kernel,
        grid=(stations // TS_ADJ,),
        in_specs=[
            pl.BlockSpec((stations, 128), lambda i: (0, 0)),
            pl.BlockSpec((2, 2, TS_ADJ, stations), lambda i: (0, 0, i, 0)),
        ],
        out_specs=pl.BlockSpec((stations, 128), lambda i: (0, 0)),
        out_shape=jax.ShapeDtypeStruct((stations, 128), jnp.float32),
        scratch_shapes=[
            pltpu.VMEM((stations, 128), jnp.bfloat16),
            pltpu.VMEM((stations, 128), jnp.float32),
        ],
    )(y, reflection)


def base_table(nfreq, ntime):
    phase = (np.arange(nfreq)[:, None] * np.arange(ntime)[None, :]) % ntime
    angle = phase.astype(np.float64) * (2.0 * math.pi / ntime)
    table = np.stack([np.cos(angle), -np.sin(angle)], 1).reshape(2 * nfreq, ntime)
    return jnp.asarray(table.astype(np.float32))


def spectra_of(traces, table, groups):
    points, stations_dev, ntime = traces.shape
    tab = table.reshape(groups, table.shape[0] // groups, ntime)
    mixed = jnp.einsum("pst,dqt->dsqp", traces, tab,
        precision=lax.Precision.HIGH,
        preferred_element_type=jnp.float32,
    )
    scaled = (mixed * (1.0 / math.sqrt(ntime))).astype(jnp.bfloat16)
    return scaled.reshape(groups, stations_dev, tab.shape[1] * points)


def traces_of(arrived, table, points):
    groups = arrived.shape[0]
    stations_dev = arrived.size // (groups * 128)
    local = 128 // (2 * points)
    spec = arrived.reshape(groups, stations_dev, local, 2, points)
    tab = table.reshape(groups, local, 2, table.shape[1])
    mixed = lax.dot_general(
        spec,
        tab,
        (((0, 2, 3), (0, 1, 2)), ((), ())),
        precision=lax.Precision.HIGH,
        preferred_element_type=jnp.float32,
    )
    scaled = mixed * (1.0 / math.sqrt(table.shape[0] // 2))
    return scaled.transpose(1, 0, 2)


def windowed(traces, onset_index):
    time_index = jnp.arange(traces.shape[2], dtype=jnp.int32)
    distance = jnp.abs(time_index - traces.shape[2] // 2)
    keep = distance[None, None, :] < onset_index[:, :, None]
    return jnp.where(keep, traces, jnp.zeros_like(traces))


def per_device(reflection, focus_plus, focus_direct, onset_index):
    groups = lax.axis_size("af")
    points = focus_plus.shape[0]
    table = base_table(NFREQ, NT)

    def convolve(spectra, product):
        arrived = lax.all_to_all(spectra, "af", 0, 0, tiled=True)
        stations = arrived.size // 128
        result = product(reflection, arrived.reshape(stations, 128))
        result = result.reshape(arrived.shape[0], 1, -1)
        return lax.all_to_all(result, "af", 0, 0, tiled=True)

    images = convolve(spectra_of(focus_plus, table, groups), forward_kernel)
    focus_minus = windowed(traces_of(images, table, points), onset_index)
    returns = convolve(spectra_of(focus_minus, table, groups), adjoint_kernel)
    focus_next = focus_direct + windowed(traces_of(returns, table, points), onset_index)
    return (focus_minus, focus_next)


def solution(mesh):
    return jax.shard_map(
        per_device,
        mesh=mesh,
        in_specs=(
            P(None, "af", None, None),
            P(None, "af", None),
            P(None, "af", None),
            P(None, "af"),
        ),
        out_specs=(P(None, "af", None), P(None, "af", None)),
        check_vma=False,
    )
```

```python
import math

import numpy as np

import jax
import jax.numpy as jnp
from jax import lax
from jax.experimental import pallas as pl
from jax.experimental.pallas import tpu as pltpu
from jax.sharding import PartitionSpec as P

NFREQ = 256
NT = 512
TS = 512


def _partner(x, negate_first):
    x = x.astype(jnp.float32)
    lane = lax.broadcasted_iota(jnp.int32, x.shape, 1)
    first = (lane % 64) < 32
    ahead = pltpu.roll(x, 96, 1)
    behind = pltpu.roll(x, 32, 1)
    if negate_first:
        out = jnp.where(first, -ahead, behind)
    else:
        out = jnp.where(first, ahead, -behind)
    return out.astype(jnp.bfloat16)


def _fwd_kernel(x_ref, r_ref, o_ref, xp_ref):
    @pl.when(pl.program_id(0) == 0)
    def _():
        xp_ref[...] = _partner(x_ref[...], True)

    parts = []
    for kl in range(2):
        x = x_ref[:, kl * 64:(kl + 1) * 64]
        xp = xp_ref[:, kl * 64:(kl + 1) * 64]
        a = jnp.dot(r_ref[0, kl], x, preferred_element_type=jnp.float32)
        a = a + jnp.dot(r_ref[1, kl], xp, preferred_element_type=jnp.float32)
        parts.append(a)
    o_ref[...] = jnp.concatenate(parts, 1)


def forward_kernel(reflection, x):
    stations = x.shape[0]
    return pl.pallas_call(
        _fwd_kernel,
        grid=(stations // TS,),
        in_specs=[
            pl.BlockSpec((stations, 128), lambda i: (0, 0)),
            pl.BlockSpec((2, 2, TS, stations), lambda i: (0, 0, i, 0)),
        ],
        out_specs=pl.BlockSpec((TS, 128), lambda i: (i, 0)),
        out_shape=jax.ShapeDtypeStruct((stations, 128), jnp.float32),
        scratch_shapes=[pltpu.VMEM((stations, 128), jnp.bfloat16)],
    )(x, reflection)


def _adj_kernel(y_ref, r_ref, o_ref, yp_ref):
    i = pl.program_id(0)

    @pl.when(i == 0)
    def _():
        yp_ref[...] = _partner(y_ref[...], False)

    off = pl.multiple_of(i * TS, TS)
    y = y_ref[pl.ds(off, TS), :]
    yp = yp_ref[pl.ds(off, TS), :]
    dims = (((0,), (0,)), ((), ()))
    parts = []
    for kl in range(2):
        a = lax.dot_general(r_ref[0, kl], y[:, kl * 64:(kl + 1) * 64], dims,
                            preferred_element_type=jnp.float32)
        a = a + lax.dot_general(r_ref[1, kl], yp[:, kl * 64:(kl + 1) * 64], dims,
                                preferred_element_type=jnp.float32)
        parts.append(a)
    total = jnp.concatenate(parts, 1)

    @pl.when(i == 0)
    def _():
        o_ref[...] = total

    @pl.when(i > 0)
    def _():
        o_ref[...] += total


def adjoint_kernel(reflection, y):
    stations = y.shape[0]
    return pl.pallas_call(
        _adj_kernel,
        grid=(stations // TS,),
        in_specs=[
            pl.BlockSpec((stations, 128), lambda i: (0, 0)),
            pl.BlockSpec((2, 2, TS, stations), lambda i: (0, 0, i, 0)),
        ],
        out_specs=pl.BlockSpec((stations, 128), lambda i: (0, 0)),
        out_shape=jax.ShapeDtypeStruct((stations, 128), jnp.float32),
        scratch_shapes=[
            pltpu.VMEM((stations, 128), jnp.bfloat16),
        ],
    )(y, reflection)


def base_table(nfreq, ntime):
    phase = (np.arange(nfreq)[:, None] * np.arange(ntime)[None, :]) % ntime
    angle = phase.astype(np.float64) * (2.0 * math.pi / ntime)
    table = np.stack([np.cos(angle), -np.sin(angle)], 1).reshape(2 * nfreq, ntime)
    return jnp.asarray(table.astype(np.float32))


def spectra_of(traces, table, groups):
    points, stations_dev, ntime = traces.shape
    tab = table.reshape(groups, table.shape[0] // groups, ntime)
    mixed = jnp.einsum("pst,dqt->dsqp", traces, tab,
        precision=lax.Precision.HIGH,
        preferred_element_type=jnp.float32,
    )
    scaled = (mixed * (1.0 / math.sqrt(ntime))).astype(jnp.bfloat16)
    return scaled.reshape(groups, stations_dev, tab.shape[1] * points)


def traces_of(arrived, table, points):
    groups = arrived.shape[0]
    stations_dev = arrived.size // (groups * 128)
    local = 128 // (2 * points)
    spec = arrived.reshape(groups, stations_dev, local, 2, points)
    tab = table.reshape(groups, local, 2, table.shape[1])
    mixed = lax.dot_general(
        spec,
        tab,
        (((0, 2, 3), (0, 1, 2)), ((), ())),
        precision=lax.Precision.HIGH,
        preferred_element_type=jnp.float32,
    )
    scaled = mixed * (1.0 / math.sqrt(table.shape[0] // 2))
    return scaled.transpose(1, 0, 2)


def windowed(traces, onset_index):
    time_index = jnp.arange(traces.shape[2], dtype=jnp.int32)
    distance = jnp.abs(time_index - traces.shape[2] // 2)
    keep = distance[None, None, :] < onset_index[:, :, None]
    return jnp.where(keep, traces, jnp.zeros_like(traces))


def per_device(reflection, focus_plus, focus_direct, onset_index):
    groups = lax.axis_size("af")
    points = focus_plus.shape[0]
    table = base_table(NFREQ, NT)

    def convolve(spectra, product):
        arrived = lax.all_to_all(spectra, "af", 0, 0, tiled=True)
        stations = arrived.size // 128
        result = product(reflection, arrived.reshape(stations, 128))
        result = result.reshape(arrived.shape[0], 1, -1)
        return lax.all_to_all(result, "af", 0, 0, tiled=True)

    images = convolve(spectra_of(focus_plus, table, groups), forward_kernel)
    focus_minus = windowed(traces_of(images, table, points), onset_index)
    returns = convolve(spectra_of(focus_minus, table, groups), adjoint_kernel)
    focus_next = focus_direct + windowed(traces_of(returns, table, points), onset_index)
    return (focus_minus, focus_next)


def solution(mesh):
    return jax.shard_map(
        per_device,
        mesh=mesh,
        in_specs=(
            P(None, "af", None, None),
            P(None, "af", None),
            P(None, "af", None),
            P(None, "af"),
        ),
        out_specs=(P(None, "af", None), P(None, "af", None)),
        check_vma=False,
    )
```

```python
import math

import numpy as np

import jax
import jax.numpy as jnp
from jax import lax
from jax.experimental import pallas as pl
from jax.experimental.pallas import tpu as pltpu
from jax.sharding import PartitionSpec as P

NFREQ = 256
NT = 512
TS = 512


def _partner(x, negate_first):
    x = x.astype(jnp.float32)
    lane = lax.broadcasted_iota(jnp.int32, x.shape, 1)
    first = (lane % 64) < 32
    ahead = pltpu.roll(x, 96, 1)
    behind = pltpu.roll(x, 32, 1)
    if negate_first:
        out = jnp.where(first, -ahead, behind)
    else:
        out = jnp.where(first, ahead, -behind)
    return out.astype(jnp.bfloat16)


def _fwd_kernel(x_ref, r_ref, o_ref):
    parts = []
    for kl in range(2):
        x = x_ref[:, kl * 64:(kl + 1) * 64]
        a = jnp.dot(r_ref[0, kl], x, preferred_element_type=jnp.float32)
        b = jnp.dot(r_ref[1, kl], x, preferred_element_type=jnp.float32)
        parts.append(a[:, 0:32] - b[:, 32:64])
        parts.append(a[:, 32:64] + b[:, 0:32])
    o_ref[...] = jnp.concatenate(parts, 1)


def forward_kernel(reflection, x):
    stations = x.shape[0]
    return pl.pallas_call(
        _fwd_kernel,
        grid=(stations // TS,),
        in_specs=[
            pl.BlockSpec((stations, 128), lambda i: (0, 0)),
            pl.BlockSpec((2, 2, TS, stations), lambda i: (0, 0, i, 0)),
        ],
        out_specs=pl.BlockSpec((TS, 128), lambda i: (i, 0)),
        out_shape=jax.ShapeDtypeStruct((stations, 128), jnp.float32),
    )(x, reflection)


def _adj_kernel(y_ref, r_ref, o_ref, yp_ref, acc_ref):
    i = pl.program_id(0)

    @pl.when(i == 0)
    def _():
        yp_ref[...] = _partner(y_ref[...], False)
        acc_ref[...] = jnp.zeros(acc_ref.shape, jnp.float32)

    off = pl.multiple_of(i * TS, TS)
    y = y_ref[pl.ds(off, TS), :]
    yp = yp_ref[pl.ds(off, TS), :]
    dims = (((0,), (0,)), ((), ()))
    parts = []
    for kl in range(2):
        a = lax.dot_general(r_ref[0, kl], y[:, kl * 64:(kl + 1) * 64], dims,
                            preferred_element_type=jnp.float32)
        a = a + lax.dot_general(r_ref[1, kl], yp[:, kl * 64:(kl + 1) * 64], dims,
                                preferred_element_type=jnp.float32)
        parts.append(a)
    acc_ref[...] += jnp.concatenate(parts, 1)

    @pl.when(i == pl.num_programs(0) - 1)
    def _():
        o_ref[...] = acc_ref[...]


def adjoint_kernel(reflection, y):
    stations = y.shape[0]
    return pl.pallas_call(
        _adj_kernel,
        grid=(stations // TS,),
        in_specs=[
            pl.BlockSpec((stations, 128), lambda i: (0, 0)),
            pl.BlockSpec((2, 2, TS, stations), lambda i: (0, 0, i, 0)),
        ],
        out_specs=pl.BlockSpec((stations, 128), lambda i: (0, 0)),
        out_shape=jax.ShapeDtypeStruct((stations, 128), jnp.float32),
        scratch_shapes=[
            pltpu.VMEM((stations, 128), jnp.bfloat16),
            pltpu.VMEM((stations, 128), jnp.float32),
        ],
    )(y, reflection)


def base_table(nfreq, ntime):
    phase = (np.arange(nfreq)[:, None] * np.arange(ntime)[None, :]) % ntime
    angle = phase.astype(np.float64) * (2.0 * math.pi / ntime)
    table = np.stack([np.cos(angle), -np.sin(angle)], 1).reshape(2 * nfreq, ntime)
    return jnp.asarray(table.astype(np.float32))


def spectra_of(traces, table, groups):
    points, stations_dev, ntime = traces.shape
    tab = table.reshape(groups, table.shape[0] // groups, ntime)
    mixed = jnp.einsum("pst,dqt->dsqp", traces, tab,
        precision=lax.Precision.HIGH,
        preferred_element_type=jnp.float32,
    )
    scaled = (mixed * (1.0 / math.sqrt(ntime))).astype(jnp.bfloat16)
    return scaled.reshape(groups, stations_dev, tab.shape[1] * points)


def traces_of(arrived, table, points):
    groups = arrived.shape[0]
    stations_dev = arrived.size // (groups * 128)
    local = 128 // (2 * points)
    spec = arrived.reshape(groups, stations_dev, local, 2, points)
    tab = table.reshape(groups, local, 2, table.shape[1])
    mixed = lax.dot_general(
        spec,
        tab,
        (((0, 2, 3), (0, 1, 2)), ((), ())),
        precision=lax.Precision.HIGH,
        preferred_element_type=jnp.float32,
    )
    scaled = mixed * (1.0 / math.sqrt(table.shape[0] // 2))
    return scaled.transpose(1, 0, 2)


def windowed(traces, onset_index):
    time_index = jnp.arange(traces.shape[2], dtype=jnp.int32)
    distance = jnp.abs(time_index - traces.shape[2] // 2)
    keep = distance[None, None, :] < onset_index[:, :, None]
    return jnp.where(keep, traces, jnp.zeros_like(traces))


def per_device(reflection, focus_plus, focus_direct, onset_index):
    groups = lax.axis_size("af")
    points = focus_plus.shape[0]
    table = base_table(NFREQ, NT)

    def convolve(spectra, product):
        arrived = lax.all_to_all(spectra, "af", 0, 0, tiled=True)
        stations = arrived.size // 128
        result = product(reflection, arrived.reshape(stations, 128))
        result = result.reshape(arrived.shape[0], 1, -1)
        return lax.all_to_all(result, "af", 0, 0, tiled=True)

    images = convolve(spectra_of(focus_plus, table, groups), forward_kernel)
    focus_minus = windowed(traces_of(images, table, points), onset_index)
    returns = convolve(spectra_of(focus_minus, table, groups), adjoint_kernel)
    focus_next = focus_direct + windowed(traces_of(returns, table, points), onset_index)
    return (focus_minus, focus_next)


def solution(mesh):
    return jax.shard_map(
        per_device,
        mesh=mesh,
        in_specs=(
            P(None, "af", None, None),
            P(None, "af", None),
            P(None, "af", None),
            P(None, "af"),
        ),
        out_specs=(P(None, "af", None), P(None, "af", None)),
        check_vma=False,
    )
```
